512 devices in a mesh: dp: 8 (over z_hi, core), seq: 64 (over z_lo, y, x).
Axes of the slice: x: 4, y: 4, z: 16 (z_hi: 4, z_lo: 4; z = z_hi * 4 + z_lo), core: 2. Of those that a mesh axis runs over, the one named last changes fastest.
Arguments:
- query: bfloat16 [8, 8192, 512], P('dp', 'seq'), may hold values from -6 to 6
- key_in: bfloat16 [8, 8192, 128], P('dp', 'seq'), may hold values from -4.5 to 4.5
- value_in: bfloat16 [8, 8192, 128], P('dp', 'seq'), may hold values from -6 to 6
- out_gain: float32 [512], replicated, may hold values from 0.1 to 1.9
- cotangent: bfloat16 [8, 8192, 512], P('dp', 'seq'), may hold values from -6 to 6
Outputs:
- attended: bfloat16 [8, 8192, 512], P('dp', 'seq')
- grad_query: bfloat16 [8, 8192, 512], P('dp', 'seq')
- grad_key: bfloat16 [8, 8192, 128], P('dp', 'seq')
- grad_value: bfloat16 [8, 8192, 128], P('dp', 'seq')
- grad_gain: float32 [512], replicated
The draws below stay inside these ranges and needn't reach their ends.
All inputs are finite; a program needn't handle non-finite values.
Results may differ from the reference program's by a relative error of at most 0.012.
The reference program's roundings to bfloat16 on the way count: a program that leaves them out, or rounds other values in their place, can miss the bound.
Values may be sent and summed in bfloat16 or wider, within the bound.
No kernel may reach another device: no remote copies, remote signals or barrier semaphores. Data moves between devices by JAX's collectives and lax.ppermute only.
A program may use at most 128 MiB of HBM per device.

```python
import math
import jax
import jax.numpy as jnp
from jax import lax

HEADS = 4
KEY = 128
VAL = 128
LEN = 8192
BATCH = 8


def draw_key_in(key, part):
    noise_key = jax.random.fold_in(key, 202)
    keys_drawn = jnp.clip(jax.random.normal(noise_key, (BATCH, LEN, KEY), jnp.float32), -4.5, 4.5)
    return keys_drawn.astype(jnp.bfloat16)


def draw_query(key, part):
    noise_key = jax.random.fold_in(key, 303)
    queries = jnp.clip(2.5 * jax.random.normal(noise_key, (BATCH, LEN, HEADS * KEY), jnp.float32), -6.0, 6.0)
    return queries.astype(jnp.bfloat16)


def steps_of(own_key, shape, cuts, low, largest):
    level, own = 1.0, jax.random.fold_in(own_key, 6)
    for position, shards_of in cuts:
        draws = jnp.exp(jax.random.uniform(jax.random.fold_in(own, position), (shards_of,), jnp.float32, low / len(cuts), largest / len(cuts)))
        level = level * jnp.repeat(draws, shape[position] // shards_of).reshape([-1 if axis == position else 1 for axis in range(len(shape))])
    return level


def scatter_about(rng, extent, spread, most, cuts=(), kind=jnp.bfloat16):
    factor_of = steps_of(rng, extent, cuts, -0.22, 0.18) if cuts else 1.0
    values = jax.random.normal(rng, extent, jnp.float32) * spread * factor_of
    return jnp.minimum(jnp.maximum(values, -most), most).astype(kind)


def setup_inputs(seed: int = 0) -> dict:
    key_of = jax.random.split(jax.random.key(seed), 6)
    return {
        "query": draw_query(jax.random.fold_in(key_of[5], 71), 0),
        "key_in": draw_key_in(jax.random.fold_in(key_of[5], 71), 0),
        "value_in": scatter_about(key_of[2], (BATCH, LEN, VAL), 1.0, 6.0, ((0, 8), (1, 64))),
        "out_gain": jnp.clip(1.0 + 0.18 * jax.random.normal(key_of[3], (HEADS * VAL,), jnp.float32), 0.1, 1.9),
        "cotangent": scatter_about(key_of[4], (BATCH, LEN, HEADS * VAL), 1.0, 6.0, ((0, 8), (1, 64))),
    }


HIGHEST_PREC = lax.Precision.HIGHEST

def one_sequence(query, key_in, value_in, cotangent, out_gain):
    length = key_in.shape[0]
    block_size = math.gcd(length, 512)
    block_count = length // block_size
    score_scale = 1.0 / math.sqrt(KEY)
    key_f32 = key_in.astype(jnp.float32)
    value_f32 = value_in.astype(jnp.float32)
    gain_grid = out_gain.reshape(HEADS, VAL)
    query_blocks = query.reshape(block_count, block_size, HEADS, KEY)
    cotan_blocks = cotangent.reshape(block_count, block_size, HEADS, VAL)

    def advance(carry, block_pair):
        key_acc, value_acc, gain_acc = carry
        query_blk, cotan_blk = block_pair
        query_f32 = query_blk.astype(jnp.float32)
        scores = jnp.einsum('qhd,kd->hqk', query_f32, key_f32, precision=HIGHEST_PREC) * score_scale
        row_top = lax.optimization_barrier(jnp.max(scores, axis=2, keepdims=True))
        expo_rows = jnp.exp(scores - row_top)
        weights = lax.optimization_barrier((expo_rows / lax.optimization_barrier(jnp.sum(expo_rows, axis=2, keepdims=True))).astype(jnp.bfloat16))
        weight_f32 = weights.astype(jnp.float32)
        out_rows = jnp.einsum('hqk,kv->qhv', weight_f32, value_f32, precision=HIGHEST_PREC)
        attended = (out_rows * gain_grid).astype(jnp.bfloat16)
        upstream = cotan_blk.astype(jnp.float32)
        gain_acc = gain_acc + lax.optimization_barrier(jnp.sum(upstream * out_rows, axis=0))
        grad_out = lax.optimization_barrier((upstream * gain_grid).astype(jnp.bfloat16))
        grad_out_f32 = grad_out.astype(jnp.float32)
        delta_rows = lax.optimization_barrier(jnp.sum(grad_out_f32 * out_rows, axis=2))
        d_prob = jnp.einsum('qhv,kv->hqk', grad_out_f32, value_f32, precision=HIGHEST_PREC)
        d_score = lax.optimization_barrier((weight_f32 * (d_prob - delta_rows.T[:, :, None])).astype(jnp.bfloat16))
        score_grad_f32 = d_score.astype(jnp.float32)
        query_grad = (jnp.einsum('hqk,kd->qhd', score_grad_f32, key_f32, precision=HIGHEST_PREC) * score_scale).astype(jnp.bfloat16)
        key_acc = key_acc + jnp.einsum('hqk,qhd->kd', score_grad_f32, query_f32, precision=HIGHEST_PREC) * score_scale
        value_acc = value_acc + jnp.einsum('hqk,qhv->kv', weight_f32, grad_out_f32, precision=HIGHEST_PREC)
        return ((key_acc, value_acc, gain_acc), (attended.reshape(block_size, HEADS * VAL), query_grad.reshape(block_size, HEADS * KEY)))
    start_carry = (jnp.zeros((length, KEY), jnp.float32), jnp.zeros((length, VAL), jnp.float32), jnp.zeros((HEADS, VAL), jnp.float32))
    final_carry, outputs = lax.scan(advance, start_carry, (query_blocks, cotan_blocks))
    key_acc, value_acc, gain_acc = final_carry
    attended = outputs[0].reshape(length, HEADS * VAL)
    grad_query = outputs[1].reshape(length, HEADS * KEY)
    return (attended, grad_query, key_acc.astype(jnp.bfloat16), value_acc.astype(jnp.bfloat16), gain_acc.reshape(HEADS * VAL))

def reference(query, key_in, value_in, out_gain, cotangent):

    def per_sequence(items):
        return one_sequence(items[0], items[1], items[2], items[3], out_gain)
    attended, grad_query, grad_key, grad_value, gain_terms = lax.map(per_sequence, (query, key_in, value_in, cotangent))
    token_total = query.shape[0] * query.shape[1]
    grad_gain = lax.optimization_barrier(jnp.sum(gain_terms, axis=0)) / math.sqrt(token_total)
    return (attended, grad_query, grad_key, grad_value, grad_gain)
```

```python
import math

import jax
import jax.numpy as jnp
from jax import lax
from jax.sharding import PartitionSpec as P

HEADS = 4
KEY = 128
VAL = 128


def to_rows(tokens, heads):
    positions = tokens.shape[0]
    width = tokens.shape[1] // heads
    return (
        tokens.reshape(positions, heads, width).transpose(1, 0, 2).reshape(heads * positions, width)
    )


def to_tokens(rows_in, heads):
    positions = rows_in.shape[0] // heads
    width = rows_in.shape[1]
    return (
        rows_in.reshape(heads, positions, width)
        .transpose(1, 0, 2)
        .reshape(positions, heads * width)
    )


def contract_first(left_mat, right_mat):
    return lax.dot_general(
        left_mat, right_mat, (((0,), (0,)), ((), ())), preferred_element_type=jnp.float32
    )


def contract_last(left_mat, right_mat):
    return lax.dot_general(
        left_mat, right_mat, (((1,), (1,)), ((), ())), preferred_element_type=jnp.float32
    )


def body(query, key_in, value_in, out_gain, cotangent):
    positions = query.shape[1]
    shards = lax.axis_size("seq")
    local_kv = jnp.concatenate([key_in[0], value_in[0]], axis=1)
    kv_all = lax.all_to_all(
        jnp.broadcast_to(local_kv[None], (shards,) + local_kv.shape),
        "seq",
        split_axis=0,
        concat_axis=0,
        tiled=True,
    ).reshape(shards * positions, KEY + VAL)
    key_mat = kv_all[:, :KEY]
    value_mat = kv_all[:, KEY:]
    length = key_mat.shape[0]
    score_scale = 1.0 / math.sqrt(KEY)
    query_rows = to_rows(query[0], HEADS)
    scores = contract_last(query_rows, key_mat) * score_scale
    row_top = jnp.max(scores, axis=1, keepdims=True)
    expo_rows = jnp.exp(scores - row_top)
    weights = (expo_rows / jnp.sum(expo_rows, axis=1, keepdims=True)).astype(jnp.bfloat16)
    out_rows = jnp.dot(weights, value_mat, preferred_element_type=jnp.float32)
    out_tokens = to_tokens(out_rows, HEADS)
    attended = (out_tokens * out_gain).astype(jnp.bfloat16)
    upstream = cotangent[0].astype(jnp.float32)
    gain_part = jnp.sum(upstream * out_tokens, axis=0)
    grad_out = (upstream * out_gain).astype(jnp.bfloat16)
    grad_rows = to_rows(grad_out, HEADS)
    delta_rows = jnp.sum(grad_rows.astype(jnp.float32) * out_rows, axis=1, keepdims=True)
    block_size = 2048
    block_starts = jnp.arange(length // block_size, dtype=jnp.int32) * block_size
    query_zero = jnp.zeros((query_rows.shape[0], KEY), jnp.float32)

    def score_grad(offset_at):
        key_part = lax.dynamic_slice_in_dim(key_mat, offset_at, block_size, 0)
        value_part = lax.dynamic_slice_in_dim(value_mat, offset_at, block_size, 0)
        weight_part = lax.dynamic_slice_in_dim(weights, offset_at, block_size, 1)
        d_prob = contract_last(grad_rows, value_part)
        d_score = (weight_part.astype(jnp.float32) * (d_prob - delta_rows)).astype(jnp.bfloat16)
        return (d_score, key_part, weight_part)

    def advance_both(query_acc, offset_at):
        d_score, key_part, weight_part = score_grad(offset_at)
        query_acc = query_acc + jnp.dot(d_score, key_part, preferred_element_type=jnp.float32)
        key_term = contract_first(d_score, query_rows) * score_scale
        value_term = contract_first(weight_part, grad_rows)
        return (query_acc, (key_term, value_term))

    query_acc, both_terms = lax.scan(advance_both, query_zero, block_starts)
    gain_rows = gain_part.reshape(HEADS, VAL)
    payload = jnp.concatenate(
        [
            both_terms[0].reshape(shards, positions, KEY),
            both_terms[1].reshape(shards, positions, VAL),
            jnp.broadcast_to(gain_rows[None], (shards, HEADS, VAL)),
        ],
        axis=1,
    )
    recv = jnp.sum(
        lax.all_to_all(payload, "seq", split_axis=0, concat_axis=0, tiled=True), axis=0
    )
    grad_key = recv[:positions]
    grad_value = recv[positions : 2 * positions]
    gain_total = lax.psum(recv[2 * positions :].reshape(HEADS * VAL), "dp")
    token_total = lax.axis_size("dp") * shards * positions
    grad_gain = gain_total / math.sqrt(token_total)
    grad_query = to_tokens(query_acc * score_scale, HEADS).astype(jnp.bfloat16)
    return (
        attended[None],
        grad_query[None],
        grad_key.astype(jnp.bfloat16)[None],
        grad_value.astype(jnp.bfloat16)[None],
        grad_gain,
    )


def solution(mesh):
    placed = (
        P("dp", "seq", None),
        P("dp", "seq", None),
        P("dp", "seq", None),
        P(),
        P("dp", "seq", None),
    )
    return jax.shard_map(
        body,
        mesh=mesh,
        in_specs=placed,
        out_specs=(
            P("dp", "seq", None),
            P("dp", "seq", None),
            P("dp", "seq", None),
            P("dp", "seq", None),
            P(),
        ),
        check_vma=False,
    )
```

```python
import math

import jax
import jax.numpy as jnp
from jax import lax
from jax.sharding import PartitionSpec as P

HEADS = 4
KEY = 128
VAL = 128


def to_rows(tokens, heads):
    positions = tokens.shape[0]
    width = tokens.shape[1] // heads
    return (
        tokens.reshape(positions, heads, width).transpose(1, 0, 2).reshape(heads * positions, width)
    )


def to_tokens(rows_in, heads):
    positions = rows_in.shape[0] // heads
    width = rows_in.shape[1]
    return (
        rows_in.reshape(heads, positions, width)
        .transpose(1, 0, 2)
        .reshape(positions, heads * width)
    )


def contract_first(left_mat, right_mat):
    return lax.dot_general(
        left_mat, right_mat, (((0,), (0,)), ((), ())), preferred_element_type=jnp.float32
    )


def contract_last(left_mat, right_mat):
    return lax.dot_general(
        left_mat, right_mat, (((1,), (1,)), ((), ())), preferred_element_type=jnp.float32
    )


def gather_seq(local, shards):
    return lax.all_to_all(
        jnp.broadcast_to(local[None], (shards,) + local.shape),
        "seq",
        split_axis=0,
        concat_axis=0,
        tiled=True,
    ).reshape(shards * local.shape[0], local.shape[1])


def reduce_seq(terms):
    return jnp.sum(lax.all_to_all(terms, "seq", split_axis=0, concat_axis=0, tiled=True), axis=0)


def body(query, key_in, value_in, out_gain, cotangent):
    positions = query.shape[1]
    shards = lax.axis_size("seq")
    groups = lax.axis_size("dp")
    key_mat = gather_seq(key_in[0], shards)
    value_mat = gather_seq(value_in[0], shards)
    score_scale = 1.0 / math.sqrt(KEY)
    query_rows = to_rows(query[0], HEADS)
    scores = contract_last(query_rows, key_mat) * score_scale
    row_top = jnp.max(scores, axis=1, keepdims=True)
    expo_rows = jnp.exp(scores - row_top)
    weights = (expo_rows / jnp.sum(expo_rows, axis=1, keepdims=True)).astype(jnp.bfloat16)
    out_rows = jnp.dot(weights, value_mat, preferred_element_type=jnp.float32)
    out_tokens = to_tokens(out_rows, HEADS)
    attended = (out_tokens * out_gain).astype(jnp.bfloat16)
    upstream = cotangent[0].astype(jnp.float32)
    gain_rows = jnp.sum(upstream * out_tokens, axis=0).reshape(HEADS, VAL)
    grad_out = (upstream * out_gain).astype(jnp.bfloat16)
    grad_rows = to_rows(grad_out, HEADS)
    delta_rows = jnp.sum(grad_rows.astype(jnp.float32) * out_rows, axis=1, keepdims=True)
    value_terms = contract_first(weights, grad_rows).reshape(shards, positions, VAL)
    value_recv = reduce_seq(
        jnp.concatenate(
            [value_terms, jnp.broadcast_to(gain_rows[None], (shards, HEADS, VAL))], axis=1
        )
    )
    grad_value = value_recv[:positions]
    gain_seq = value_recv[positions:]
    gain_total = jnp.sum(
        lax.all_to_all(
            jnp.broadcast_to(gain_seq[None], (groups,) + gain_seq.shape),
            "dp",
            split_axis=0,
            concat_axis=0,
            tiled=True,
        ),
        axis=0,
    ).reshape(HEADS * VAL)
    grad_gain = gain_total / math.sqrt(groups * shards * positions)
    d_prob = contract_last(grad_rows, value_mat)
    d_score = (weights.astype(jnp.float32) * (d_prob - delta_rows)).astype(jnp.bfloat16)
    query_acc = jnp.dot(d_score, key_mat, preferred_element_type=jnp.float32)
    key_terms = (contract_first(d_score, query_rows) * score_scale).reshape(shards, positions, KEY)
    grad_key = reduce_seq(key_terms)
    grad_query = to_tokens(query_acc * score_scale, HEADS).astype(jnp.bfloat16)
    return (
        attended[None],
        grad_query[None],
        grad_key.astype(jnp.bfloat16)[None],
        grad_value.astype(jnp.bfloat16)[None],
        grad_gain,
    )


def solution(mesh):
    placed = (
        P("dp", "seq", None),
        P("dp", "seq", None),
        P("dp", "seq", None),
        P(),
        P("dp", "seq", None),
    )
    return jax.shard_map(
        body,
        mesh=mesh,
        in_specs=placed,
        out_specs=(
            P("dp", "seq", None),
            P("dp", "seq", None),
            P("dp", "seq", None),
            P("dp", "seq", None),
            P(),
        ),
        check_vma=False,
    )
```

```python
import math

import jax
import jax.numpy as jnp
from jax import lax
from jax.sharding import Mesh, PartitionSpec as P

HEADS = 4
KEY = 128
VAL = 128


def to_rows(tokens, heads):
    positions = tokens.shape[0]
    width = tokens.shape[1] // heads
    return (
        tokens.reshape(positions, heads, width).transpose(1, 0, 2).reshape(heads * positions, width)
    )


def to_tokens(rows_in, heads):
    positions = rows_in.shape[0] // heads
    width = rows_in.shape[1]
    return (
        rows_in.reshape(heads, positions, width)
        .transpose(1, 0, 2)
        .reshape(positions, heads * width)
    )


def contract_first(left_mat, right_mat):
    return lax.dot_general(
        left_mat, right_mat, (((0,), (0,)), ((), ())), preferred_element_type=jnp.float32
    )


def contract_last(left_mat, right_mat):
    return lax.dot_general(
        left_mat, right_mat, (((1,), (1,)), ((), ())), preferred_element_type=jnp.float32
    )


def gather_seq(local, shards):
    return lax.all_to_all(
        jnp.broadcast_to(local[None], (shards,) + local.shape),
        SEQ_AXES,
        split_axis=0,
        concat_axis=0,
        tiled=True,
    ).reshape(shards * local.shape[0], local.shape[1])


def reduce_seq(terms):
    return jnp.sum(lax.all_to_all(terms, SEQ_AXES, split_axis=0, concat_axis=0, tiled=True), axis=0)


SEQ_AXES = ("sz", "sy", "sx")


def scatter_seq(terms, sides):
    grid = terms.reshape(sides + (-1,) + terms.shape[1:])
    for depth in range(len(sides) - 1, -1, -1):
        grid = jnp.moveaxis(grid, depth, 0)
        grid = lax.psum_scatter(grid, SEQ_AXES[depth], scatter_dimension=0, tiled=True)[0]
    return grid


def body(query, key_in, value_in, out_gain, cotangent):
    positions = query.shape[1]
    shards = lax.axis_size(SEQ_AXES)
    sides = tuple(lax.axis_size(name) for name in SEQ_AXES)
    groups = lax.axis_size("dp")
    key_mat = gather_seq(key_in[0], shards)
    value_mat = gather_seq(value_in[0], shards)
    score_scale = 1.0 / math.sqrt(KEY)
    query_rows = to_rows(query[0], HEADS)
    scores = contract_last(query_rows, key_mat) * score_scale
    row_top = jnp.max(scores, axis=1, keepdims=True)
    expo_rows = jnp.exp(scores - row_top)
    weights = (expo_rows / jnp.sum(expo_rows, axis=1, keepdims=True)).astype(jnp.bfloat16)
    out_rows = jnp.dot(weights, value_mat, preferred_element_type=jnp.float32)
    out_tokens = to_tokens(out_rows, HEADS)
    attended = (out_tokens * out_gain).astype(jnp.bfloat16)
    upstream = cotangent[0].astype(jnp.float32)
    gain_rows = jnp.sum(upstream * out_tokens, axis=0).reshape(HEADS, VAL)
    grad_out = (upstream * out_gain).astype(jnp.bfloat16)
    grad_rows = to_rows(grad_out, HEADS)
    delta_rows = jnp.sum(grad_rows.astype(jnp.float32) * out_rows, axis=1, keepdims=True)
    gain_dp = jnp.sum(
        lax.all_to_all(
            jnp.broadcast_to(gain_rows[None], (groups,) + gain_rows.shape),
            "dp",
            split_axis=0,
            concat_axis=0,
            tiled=True,
        ),
        axis=0,
    )
    value_terms = contract_first(weights, grad_rows)
    grad_value = scatter_seq(value_terms, sides)
    d_prob = contract_last(grad_rows, value_mat)
    d_score = (weights.astype(jnp.float32) * (d_prob - delta_rows)).astype(jnp.bfloat16)
    query_acc = jnp.dot(d_score, key_mat, preferred_element_type=jnp.float32)
    key_terms = (contract_first(d_score, query_rows) * score_scale).reshape(shards, positions, KEY)
    key_recv = reduce_seq(
        jnp.concatenate([key_terms, jnp.broadcast_to(gain_dp[None], (shards, HEADS, KEY))], axis=1)
    )
    grad_key = key_recv[:positions]
    grad_gain = key_recv[positions:].reshape(HEADS * VAL) / math.sqrt(groups * shards * positions)
    grad_query = to_tokens(query_acc * score_scale, HEADS).astype(jnp.bfloat16)
    return (
        attended[None],
        grad_query[None],
        grad_key.astype(jnp.bfloat16)[None],
        grad_value.astype(jnp.bfloat16)[None],
        grad_gain,
    )


def solution(mesh):
    sides = (4, 4, 4) if mesh.shape["seq"] == 64 else None
    split_mesh = Mesh(
        mesh.devices.reshape((mesh.shape["dp"],) + sides), ("dp",) + SEQ_AXES
    )
    tokens = P("dp", SEQ_AXES, None)
    placed = (tokens, tokens, tokens, P(), tokens)
    return jax.shard_map(
        body,
        mesh=split_mesh,
        in_specs=placed,
        out_specs=(tokens, tokens, tokens, tokens, P()),
        check_vma=False,
    )
```

```python
import math

import jax
import jax.numpy as jnp
from jax import lax
from jax.sharding import PartitionSpec as P

HEADS = 4
KEY = 128
VAL = 128


def to_rows(tokens, heads):
    positions = tokens.shape[0]
    width = tokens.shape[1] // heads
    return (
        tokens.reshape(positions, heads, width).transpose(1, 0, 2).reshape(heads * positions, width)
    )


def to_tokens(rows_in, heads):
    positions = rows_in.shape[0] // heads
    width = rows_in.shape[1]
    return (
        rows_in.reshape(heads, positions, width)
        .transpose(1, 0, 2)
        .reshape(positions, heads * width)
    )


def contract_first(left_mat, right_mat):
    return lax.dot_general(
        left_mat, right_mat, (((0,), (0,)), ((), ())), preferred_element_type=jnp.float32
    )


def contract_last(left_mat, right_mat):
    return lax.dot_general(
        left_mat, right_mat, (((1,), (1,)), ((), ())), preferred_element_type=jnp.float32
    )


def gather_seq(local, shards):
    return lax.all_to_all(
        jnp.broadcast_to(local[None], (shards,) + local.shape),
        "seq",
        split_axis=0,
        concat_axis=0,
        tiled=True,
    ).reshape(shards * local.shape[0], local.shape[1])


def reduce_seq(terms):
    return jnp.sum(lax.all_to_all(terms, "seq", split_axis=0, concat_axis=0, tiled=True), axis=0)


def body(query, key_in, value_in, out_gain, cotangent):
    positions = query.shape[1]
    shards = lax.axis_size("seq")
    groups = lax.axis_size("dp")
    key_mat = gather_seq(key_in[0], shards)
    value_mat = gather_seq(value_in[0], shards)
    score_scale = 1.0 / math.sqrt(KEY)
    query_rows = to_rows(query[0], HEADS)
    scores = contract_last(query_rows, key_mat) * score_scale
    row_top = jnp.max(scores, axis=1, keepdims=True)
    expo_rows = jnp.exp(scores - row_top)
    weights = (expo_rows / jnp.sum(expo_rows, axis=1, keepdims=True)).astype(jnp.bfloat16)
    out_rows = jnp.dot(weights, value_mat, preferred_element_type=jnp.float32)
    out_tokens = to_tokens(out_rows, HEADS)
    attended = (out_tokens * out_gain).astype(jnp.bfloat16)
    upstream = cotangent[0].astype(jnp.float32)
    gain_rows = jnp.sum(upstream * out_tokens, axis=0).reshape(HEADS, VAL)
    grad_out = (upstream * out_gain).astype(jnp.bfloat16)
    grad_rows = to_rows(grad_out, HEADS)
    delta_rows = jnp.sum(grad_rows.astype(jnp.float32) * out_rows, axis=1, keepdims=True)
    value_terms = contract_first(weights, grad_rows).reshape(shards, positions, VAL)
    grad_value = reduce_seq(value_terms)
    d_prob = contract_last(grad_rows, value_mat)
    d_score = (weights.astype(jnp.float32) * (d_prob - delta_rows)).astype(jnp.bfloat16)
    query_acc = jnp.dot(d_score, key_mat, preferred_element_type=jnp.float32)
    key_terms = (contract_first(d_score, query_rows) * score_scale).reshape(shards, positions, KEY)
    key_recv = reduce_seq(
        jnp.concatenate([key_terms, jnp.broadcast_to(gain_rows[None], (shards, HEADS, KEY))], axis=1)
    )
    grad_key = key_recv[:positions]
    gain_seq = key_recv[positions:]
    gain_total = jnp.sum(
        lax.all_to_all(
            jnp.broadcast_to(gain_seq[None], (groups,) + gain_seq.shape),
            "dp",
            split_axis=0,
            concat_axis=0,
            tiled=True,
        ),
        axis=0,
    ).reshape(HEADS * VAL)
    grad_gain = gain_total / math.sqrt(groups * shards * positions)
    grad_query = to_tokens(query_acc * score_scale, HEADS).astype(jnp.bfloat16)
    return (
        attended[None],
        grad_query[None],
        grad_key.astype(jnp.bfloat16)[None],
        grad_value.astype(jnp.bfloat16)[None],
        grad_gain,
    )


def solution(mesh):
    placed = (
        P("dp", "seq", None),
        P("dp", "seq", None),
        P("dp", "seq", None),
        P(),
        P("dp", "seq", None),
    )
    return jax.shard_map(
        body,
        mesh=mesh,
        in_specs=placed,
        out_specs=(
            P("dp", "seq", None),
            P("dp", "seq", None),
            P("dp", "seq", None),
            P("dp", "seq", None),
            P(),
        ),
        check_vma=False,
    )
```

```python
import math

import jax
import jax.numpy as jnp
from jax import lax
from jax.sharding import PartitionSpec as P

HEADS = 4
KEY = 128
VAL = 128


def to_rows(tokens, heads):
    positions = tokens.shape[0]
    width = tokens.shape[1] // heads
    return (
        tokens.reshape(positions, heads, width).transpose(1, 0, 2).reshape(heads * positions, width)
    )


def to_tokens(rows_in, heads):
    positions = rows_in.shape[0] // heads
    width = rows_in.shape[1]
    return (
        rows_in.reshape(heads, positions, width)
        .transpose(1, 0, 2)
        .reshape(positions, heads * width)
    )


def contract_first(left_mat, right_mat):
    return lax.dot_general(
        left_mat, right_mat, (((0,), (0,)), ((), ())), preferred_element_type=jnp.float32
    )


def contract_last(left_mat, right_mat):
    return lax.dot_general(
        left_mat, right_mat, (((1,), (1,)), ((), ())), preferred_element_type=jnp.float32
    )


def gather_seq(local, shards):
    return lax.all_to_all(
        jnp.broadcast_to(local[None], (shards,) + local.shape),
        "seq",
        split_axis=0,
        concat_axis=0,
        tiled=True,
    ).reshape(shards * local.shape[0], local.shape[1])


def reduce_seq(terms):
    recv = lax.all_to_all(terms, "seq", split_axis=0, concat_axis=0, tiled=True)
    return jnp.sum(recv.astype(jnp.float32), axis=0)


def body(query, key_in, value_in, out_gain, cotangent):
    positions = query.shape[1]
    shards = lax.axis_size("seq")
    groups = lax.axis_size("dp")
    key_mat = gather_seq(key_in[0], shards)
    value_mat = gather_seq(value_in[0], shards)
    score_scale = 1.0 / math.sqrt(KEY)
    query_rows = to_rows(query[0], HEADS)
    scores = contract_last(query_rows, key_mat) * score_scale
    row_top = jnp.max(scores, axis=1, keepdims=True)
    expo_rows = jnp.exp(scores - row_top)
    weights = (expo_rows / jnp.sum(expo_rows, axis=1, keepdims=True)).astype(jnp.bfloat16)
    out_rows = jnp.dot(weights, value_mat, preferred_element_type=jnp.float32)
    out_tokens = to_tokens(out_rows, HEADS)
    attended = (out_tokens * out_gain).astype(jnp.bfloat16)
    upstream = cotangent[0].astype(jnp.float32)
    gain_rows = jnp.sum(upstream * out_tokens, axis=0).reshape(HEADS, VAL)
    grad_out = (upstream * out_gain).astype(jnp.bfloat16)
    grad_rows = to_rows(grad_out, HEADS)
    delta_rows = jnp.sum(grad_rows.astype(jnp.float32) * out_rows, axis=1, keepdims=True)
    value_terms = contract_first(weights, grad_rows).reshape(shards, positions, VAL).astype(jnp.bfloat16)
    grad_value = reduce_seq(value_terms)
    d_prob = contract_last(grad_rows, value_mat)
    d_score = (weights.astype(jnp.float32) * (d_prob - delta_rows)).astype(jnp.bfloat16)
    query_acc = jnp.dot(d_score, key_mat, preferred_element_type=jnp.float32)
    key_terms = (contract_first(d_score, query_rows) * score_scale).reshape(shards, positions, KEY)
    gain_high = gain_rows.astype(jnp.bfloat16)
    gain_low = (gain_rows - gain_high.astype(jnp.float32)).astype(jnp.bfloat16)
    gain_pair = jnp.concatenate([gain_high, gain_low], axis=0)
    key_recv = reduce_seq(
        jnp.concatenate(
            [
                key_terms.astype(jnp.bfloat16),
                jnp.broadcast_to(gain_pair[None], (shards, 2 * HEADS, KEY)),
            ],
            axis=1,
        )
    )
    grad_key = key_recv[:positions]
    gain_seq = key_recv[positions : positions + HEADS] + key_recv[positions + HEADS :]
    gain_total = jnp.sum(
        lax.all_to_all(
            jnp.broadcast_to(gain_seq[None], (groups,) + gain_seq.shape),
            "dp",
            split_axis=0,
            concat_axis=0,
            tiled=True,
        ),
        axis=0,
    ).reshape(HEADS * VAL)
    grad_gain = gain_total / math.sqrt(groups * shards * positions)
    grad_query = to_tokens(query_acc * score_scale, HEADS).astype(jnp.bfloat16)
    return (
        attended[None],
        grad_query[None],
        grad_key.astype(jnp.bfloat16)[None],
        grad_value.astype(jnp.bfloat16)[None],
        grad_gain,
    )


def solution(mesh):
    placed = (
        P("dp", "seq", None),
        P("dp", "seq", None),
        P("dp", "seq", None),
        P(),
        P("dp", "seq", None),
    )
    return jax.shard_map(
        body,
        mesh=mesh,
        in_specs=placed,
        out_specs=(
            P("dp", "seq", None),
            P("dp", "seq", None),
            P("dp", "seq", None),
            P("dp", "seq", None),
            P(),
        ),
        check_vma=False,
    )
```

```python
import math

import jax
import jax.numpy as jnp
from jax import lax
from jax.sharding import PartitionSpec as P

HEADS = 4
KEY = 128
VAL = 128


def to_rows(tokens, heads):
    positions = tokens.shape[0]
    width = tokens.shape[1] // heads
    return (
        tokens.reshape(positions, heads, width).transpose(1, 0, 2).reshape(heads * positions, width)
    )


def to_tokens(rows_in, heads):
    positions = rows_in.shape[0] // heads
    width = rows_in.shape[1]
    return (
        rows_in.reshape(heads, positions, width)
        .transpose(1, 0, 2)
        .reshape(positions, heads * width)
    )


def contract_first(left_mat, right_mat):
    return lax.dot_general(
        left_mat, right_mat, (((0,), (0,)), ((), ())), preferred_element_type=jnp.float32
    )


def contract_last(left_mat, right_mat):
    return lax.dot_general(
        left_mat, right_mat, (((1,), (1,)), ((), ())), preferred_element_type=jnp.float32
    )


def gather_seq(local, shards):
    return lax.all_to_all(
        jnp.broadcast_to(local[None], (shards,) + local.shape),
        "seq",
        split_axis=0,
        concat_axis=0,
        tiled=True,
    ).reshape(shards * local.shape[0], local.shape[1])


def reduce_seq(terms):
    recv = lax.all_to_all(terms, "seq", split_axis=0, concat_axis=0, tiled=True)
    return jnp.sum(recv.astype(jnp.float32), axis=0)


def body(query, key_in, value_in, out_gain, cotangent):
    positions = query.shape[1]
    shards = lax.axis_size("seq")
    groups = lax.axis_size("dp")
    key_mat = gather_seq(key_in[0], shards)
    value_mat = gather_seq(value_in[0], shards)
    score_scale = 1.0 / math.sqrt(KEY)
    query_rows = to_rows(query[0], HEADS)
    scores = contract_last(query_rows, key_mat) * score_scale
    row_top = jnp.max(scores, axis=1, keepdims=True)
    expo_rows = jnp.exp(scores - row_top)
    weights = (expo_rows / jnp.sum(expo_rows, axis=1, keepdims=True)).astype(jnp.bfloat16)
    out_rows = jnp.dot(weights, value_mat, preferred_element_type=jnp.float32)
    out_tokens = to_tokens(out_rows, HEADS)
    attended = (out_tokens * out_gain).astype(jnp.bfloat16)
    upstream = cotangent[0].astype(jnp.float32)
    gain_rows = jnp.sum(upstream * out_tokens, axis=0).reshape(HEADS, VAL)
    grad_out = (upstream * out_gain).astype(jnp.bfloat16)
    grad_rows = to_rows(grad_out, HEADS)
    delta_rows = jnp.sum(grad_rows.astype(jnp.float32) * out_rows, axis=1, keepdims=True)
    value_terms = contract_first(weights, grad_rows).reshape(shards, positions, VAL).astype(jnp.bfloat16)
    grad_value = reduce_seq(value_terms)
    d_prob = contract_last(grad_rows, value_mat)
    d_score = (weights.astype(jnp.float32) * (d_prob - delta_rows)).astype(jnp.bfloat16)
    query_acc = jnp.dot(d_score, key_mat, preferred_element_type=jnp.float32)
    key_terms = (contract_first(d_score, query_rows) * score_scale).reshape(shards, positions, KEY)
    gain_rows = lax.psum(gain_rows, "dp")
    gain_high = gain_rows.astype(jnp.bfloat16)
    gain_low = (gain_rows - gain_high.astype(jnp.float32)).astype(jnp.bfloat16)
    gain_pair = jnp.concatenate([gain_high, gain_low], axis=0)
    key_recv = reduce_seq(
        jnp.concatenate(
            [
                key_terms.astype(jnp.bfloat16),
                jnp.broadcast_to(gain_pair[None], (shards, 2 * HEADS, KEY)),
            ],
            axis=1,
        )
    )
    grad_key = key_recv[:positions]
    gain_seq = key_recv[positions : positions + HEADS] + key_recv[positions + HEADS :]
    gain_total = gain_seq.reshape(HEADS * VAL)
    grad_gain = gain_total / math.sqrt(groups * shards * positions)
    grad_query = to_tokens(query_acc * score_scale, HEADS).astype(jnp.bfloat16)
    return (
        attended[None],
        grad_query[None],
        grad_key.astype(jnp.bfloat16)[None],
        grad_value.astype(jnp.bfloat16)[None],
        grad_gain,
    )


def solution(mesh):
    placed = (
        P("dp", "seq", None),
        P("dp", "seq", None),
        P("dp", "seq", None),
        P(),
        P("dp", "seq", None),
    )
    return jax.shard_map(
        body,
        mesh=mesh,
        in_specs=placed,
        out_specs=(
            P("dp", "seq", None),
            P("dp", "seq", None),
            P("dp", "seq", None),
            P("dp", "seq", None),
            P(),
        ),
        check_vma=False,
    )
```

```python
import math

import jax
import jax.numpy as jnp
from jax import lax
from jax.sharding import PartitionSpec as P


HEADS = 4
KEY = 128
VAL = 128


def to_rows(tokens, heads):
    positions = tokens.shape[0]
    width = tokens.shape[1] // heads
    return (
        tokens.reshape(positions, heads, width).transpose(1, 0, 2).reshape(heads * positions, width)
    )


def to_tokens(rows_in, heads):
    positions = rows_in.shape[0] // heads
    width = rows_in.shape[1]
    return (
        rows_in.reshape(heads, positions, width)
        .transpose(1, 0, 2)
        .reshape(positions, heads * width)
    )


def contract_first(left_mat, right_mat):
    return lax.dot_general(
        left_mat, right_mat, (((0,), (0,)), ((), ())), preferred_element_type=jnp.float32
    )


def contract_last(left_mat, right_mat):
    return lax.dot_general(
        left_mat, right_mat, (((1,), (1,)), ((), ())), preferred_element_type=jnp.float32
    )


def gather_seq(local, shards):
    return lax.all_to_all(
        jnp.broadcast_to(local[None], (shards,) + local.shape),
        "seq",
        split_axis=0,
        concat_axis=0,
        tiled=True,
    ).reshape(shards * local.shape[0], local.shape[1])


def reduce_seq(terms):
    recv = lax.all_to_all(terms, "seq", split_axis=0, concat_axis=0, tiled=True)
    return jnp.sum(recv.astype(jnp.float32), axis=0)


def layer(query, key_in, value_in, out_gain, cotangent):
    positions = query.shape[1]
    shards = lax.axis_size("seq")
    groups = lax.axis_size("dp")
    key_mat = gather_seq(key_in[0], shards)
    value_mat = gather_seq(value_in[0], shards)
    score_scale = 1.0 / math.sqrt(KEY)
    query_rows = to_rows(query[0], HEADS)
    scores = contract_last(query_rows, key_mat) * score_scale
    row_top = jnp.max(scores, axis=1, keepdims=True)
    expo_rows = jnp.exp(scores - row_top)
    weights = (expo_rows / jnp.sum(expo_rows, axis=1, keepdims=True)).astype(jnp.bfloat16)
    out_rows = jnp.dot(weights, value_mat, preferred_element_type=jnp.float32)
    out_tokens = to_tokens(out_rows, HEADS)
    attended = (out_tokens * out_gain).astype(jnp.bfloat16)
    upstream = cotangent[0].astype(jnp.float32)
    gain_rows = jnp.sum(upstream * out_tokens, axis=0).reshape(HEADS, VAL)
    grad_out = (upstream * out_gain).astype(jnp.bfloat16)
    grad_rows = to_rows(grad_out, HEADS)
    delta_rows = jnp.sum(grad_rows.astype(jnp.float32) * out_rows, axis=1, keepdims=True)
    value_terms = contract_first(weights, grad_rows)
    value_terms = value_terms.reshape(shards, positions, VAL).astype(jnp.bfloat16)
    gain_high = gain_rows.astype(jnp.bfloat16)
    gain_low = (gain_rows - gain_high.astype(jnp.float32)).astype(jnp.bfloat16)
    gain_pair = jnp.concatenate([gain_high, gain_low], axis=0)
    value_recv = reduce_seq(
        jnp.concatenate(
            [value_terms, jnp.broadcast_to(gain_pair[None], (shards, 2 * HEADS, VAL))], axis=1
        )
    )
    grad_value = value_recv[:positions]
    gain_seq = value_recv[positions : positions + HEADS] + value_recv[positions + HEADS :]
    d_prob = contract_last(grad_rows, value_mat)
    d_score = (weights.astype(jnp.float32) * (d_prob - delta_rows)).astype(jnp.bfloat16)
    query_acc = jnp.dot(d_score, key_mat, preferred_element_type=jnp.float32)
    key_terms = (contract_first(d_score, query_rows) * score_scale).reshape(shards, positions, KEY)
    grad_key = reduce_seq(key_terms.astype(jnp.bfloat16))
    gain_total = lax.psum(gain_seq, "dp")
    gain_total = gain_total.reshape(HEADS * VAL)
    grad_gain = gain_total / math.sqrt(groups * shards * positions)
    grad_query = to_tokens(query_acc * score_scale, HEADS).astype(jnp.bfloat16)
    return (
        attended[None],
        grad_query[None],
        grad_key.astype(jnp.bfloat16)[None],
        grad_value.astype(jnp.bfloat16)[None],
        grad_gain,
    )


def solution(mesh):
    placed = (
        P("dp", "seq", None),
        P("dp", "seq", None),
        P("dp", "seq", None),
        P(),
        P("dp", "seq", None),
    )
    return jax.shard_map(
        layer,
        mesh=mesh,
        in_specs=placed,
        out_specs=(
            P("dp", "seq", None),
            P("dp", "seq", None),
            P("dp", "seq", None),
            P("dp", "seq", None),
            P(),
        ),
        check_vma=False,
    )
```
